128 devices in a mesh: row: 32 (over x_lo, z, y), col: 4 (over x_hi, core).
Axes of the slice: x: 4 (x_hi: 2, x_lo: 2; x = x_hi * 2 + x_lo), y: 4, z: 4, core: 2. Of those that a mesh axis runs over, the one named last changes fastest.
Arguments:
- inputs: bfloat16 [1024, 8192], P('row', 'col'), may hold values from -6 to 6
- out_grad: bfloat16 [1024, 8192], P('row', 'col'), may hold values from -4 to 4
- gate_pre: bfloat16 [1024, 28672], P('col', 'row'), may hold values from -6 to 6
- up_pre: bfloat16 [1024, 28672], P('col', 'row'), may hold values from -6 to 6
- gate_weight: bfloat16 [8192, 28672], P('col', 'row'), may hold values from -0.0625 to 0.0625
- up_weight: bfloat16 [8192, 28672], P('col', 'row'), may hold values from -0.0625 to 0.0625
- down_weight: bfloat16 [28672, 8192], P('row', 'col'), may hold values from -0.03125 to 0.03125
Outputs:
- grad_input: bfloat16 [1024, 8192], P('row', 'col')
- grad_gate: bfloat16 [8192, 28672], P('col', 'row')
- grad_up: bfloat16 [8192, 28672], P('col', 'row')
- grad_down: bfloat16 [28672, 8192], P('row', 'col')
The draws below stay inside these ranges and needn't reach their ends.
All inputs are finite; a program needn't handle non-finite values.
Results may differ from the reference program's by a relative error of at most 0.005.
Values may be sent and summed in bfloat16 or wider, within the bound.
No kernel may reach another device: no remote copies, remote signals or barrier semaphores. Data moves between devices by JAX's collectives and lax.ppermute only.
A program may use at most 128 MiB of HBM per device.

```python
import jax
import jax.numpy as jnp

D = 8192
FF = 28672
TOKENS = 1024


def steps_of(rng, dims, cuts, least, largest):
    def one(position, blocks):
        heights = jax.random.uniform(jax.random.fold_in(jax.random.fold_in(rng, 6), position), (blocks,), jnp.float32, least / len(cuts), largest / len(cuts))
        return jnp.repeat(jnp.exp(heights), dims[position] // blocks).reshape((-1,) + (1,) * (len(dims) - position - 1))

    factor_of = one(*cuts[0])
    for cut in cuts[1:]:
        factor_of = factor_of * one(*cut)
    return factor_of


def bell_draw(stream_key, dims, spread, limit, pieces=(), dtype=jnp.bfloat16):
    level = steps_of(stream_key, dims, pieces, -0.22, 0.18) if pieces else 1.0
    drawn = jax.random.normal(stream_key, dims, jnp.float32) * spread * level
    return jnp.minimum(jnp.maximum(drawn, -limit), limit).astype(dtype)


def setup_inputs(seed: int = 0) -> dict:
    seeds = jax.random.split(jax.random.key(seed), 8)
    inputs = bell_draw(seeds[0], (TOKENS, D), 0.5, 6.0, ((0, 32), (1, 4)))
    out_grad = bell_draw(seeds[1], (TOKENS, D), (8.0 / TOKENS ** 0.5), 4.0, ((0, 32), (1, 4)))
    gate_pre = bell_draw(seeds[2], (TOKENS, FF), 1.5, 6.0, ((0, 4), (1, 32)))
    up_pre = bell_draw(seeds[3], (TOKENS, FF), 1.0, 6.0, ((0, 4), (1, 32)))
    gate_weight = bell_draw(seeds[4], (D, FF), D ** -0.5, 0.0625, ((0, 4), (1, 32)))
    up_weight = bell_draw(seeds[5], (D, FF), D ** -0.5, 0.0625, ((0, 4), (1, 32)))
    down_weight = bell_draw(seeds[6], (FF, D), FF ** -0.5, 0.03125, ((0, 32), (1, 4)))
    return dict(inputs=inputs, out_grad=out_grad, gate_pre=gate_pre, up_pre=up_pre, gate_weight=gate_weight, up_weight=up_weight, down_weight=down_weight)


def reference(inputs, out_grad, gate_pre, up_pre, gate_weight, up_weight, down_weight):
    hidden_grad = jnp.dot(out_grad, down_weight.T, preferred_element_type=jnp.float32)
    gate_value = gate_pre.astype(jnp.float32)
    up_value = up_pre.astype(jnp.float32)
    sigmoid_gate = jax.nn.sigmoid(gate_value)
    activated = gate_value * sigmoid_gate
    hidden = (activated * up_value).astype(jnp.bfloat16)
    gate_grad = (hidden_grad * up_value * sigmoid_gate * (1.0 + gate_value * (1.0 - sigmoid_gate))).astype(jnp.bfloat16)
    up_grad = (hidden_grad * activated).astype(jnp.bfloat16)
    grad_down = jnp.dot(hidden.T, out_grad, preferred_element_type=jnp.float32).astype(jnp.bfloat16)
    grad_gate = jnp.dot(inputs.T, gate_grad, preferred_element_type=jnp.float32).astype(jnp.bfloat16)
    grad_up = jnp.dot(inputs.T, up_grad, preferred_element_type=jnp.float32).astype(jnp.bfloat16)
    total = jnp.dot(gate_grad, gate_weight.T, preferred_element_type=jnp.float32)
    total = total + jnp.dot(up_grad, up_weight.T, preferred_element_type=jnp.float32)
    grad_input = total.astype(jnp.bfloat16)
    return (grad_input, grad_gate, grad_up, grad_down)
```

```python
import jax
import jax.numpy as jnp
from jax import lax
from jax.sharding import PartitionSpec as P


def swiglu_back(hidden_grad, gate_stored, up_stored):
    gate_value = gate_stored.astype(jnp.float32)
    up_value = up_stored.astype(jnp.float32)
    sigmoid_gate = jax.nn.sigmoid(gate_value)
    activated = gate_value * sigmoid_gate
    hidden = (activated * up_value).astype(jnp.bfloat16)
    gate_grad = (
        hidden_grad * up_value * sigmoid_gate * (1.0 + gate_value * (1.0 - sigmoid_gate))
    ).astype(jnp.bfloat16)
    up_grad = (hidden_grad * activated).astype(jnp.bfloat16)
    return (hidden, gate_grad, up_grad)


def contract_last(left, right):
    return lax.dot_general(
        left, right, (((1,), (1,)), ((), ())), preferred_element_type=jnp.float32
    )


def contract_first(left, right):
    return lax.dot_general(
        left, right, (((0,), (0,)), ((), ())), preferred_element_type=jnp.float32
    )


def gather_rows(block, axis, count):
    tiled = jnp.tile(block, (count, 1))
    return lax.all_to_all(tiled, axis, 0, 0, tiled=True)


def scatter_sum_rows(partial, axis, count):
    received = lax.all_to_all(partial, axis, 0, 0, tiled=True)
    return received.reshape((count, partial.shape[0] // count) + partial.shape[1:]).sum(0)


def make_body(rows):
    def body(inputs, out_grad, gate_pre, up_pre, gate_weight, up_weight, down_weight):
        grad_rows = gather_rows(out_grad, "row", rows)
        width = gate_pre.shape[1]
        pre_all = lax.all_gather(
            jnp.concatenate([gate_pre, up_pre], axis=1), "col", axis=0, tiled=True
        )
        gate_all, up_all = pre_all[:, :width], pre_all[:, width:]
        partial_hidden = contract_last(grad_rows, down_weight)
        hidden_total = lax.psum(partial_hidden, "col")
        hidden, gate_grad, up_grad = swiglu_back(hidden_total, gate_all, up_all)
        grad_down = contract_first(hidden, grad_rows).astype(jnp.bfloat16)
        input_rows = gather_rows(inputs, "row", rows)
        gate_total = contract_first(input_rows, gate_grad)
        up_total = contract_first(input_rows, up_grad)
        input_total = scatter_sum_rows(
            contract_last(gate_grad, gate_weight) + contract_last(up_grad, up_weight),
            "row",
            rows,
        )
        return (
            input_total.astype(jnp.bfloat16),
            gate_total.astype(jnp.bfloat16),
            up_total.astype(jnp.bfloat16),
            grad_down,
        )

    return body


def solution(mesh):
    in_specs = (
        P("row", "col"),
        P("row", "col"),
        P("col", "row"),
        P("col", "row"),
        P("col", "row"),
        P("col", "row"),
        P("row", "col"),
    )
    out_specs = (P("row", "col"), P("col", "row"), P("col", "row"), P("row", "col"))
    body = make_body(mesh.shape["row"])
    return jax.shard_map(body, mesh=mesh, in_specs=in_specs, out_specs=out_specs, check_vma=False)
```

```python
import jax
import jax.numpy as jnp
from jax import lax
from jax.sharding import PartitionSpec as P


def swiglu_back(hidden_grad, gate_stored, up_stored):
    gate_value = gate_stored.astype(jnp.float32)
    up_value = up_stored.astype(jnp.float32)
    sigmoid_gate = jax.nn.sigmoid(gate_value)
    activated = gate_value * sigmoid_gate
    hidden = (activated * up_value).astype(jnp.bfloat16)
    gate_grad = (
        hidden_grad * up_value * sigmoid_gate * (1.0 + gate_value * (1.0 - sigmoid_gate))
    ).astype(jnp.bfloat16)
    up_grad = (hidden_grad * activated).astype(jnp.bfloat16)
    return (hidden, gate_grad, up_grad)


def contract_last(left, right):
    return lax.dot_general(
        left, right, (((1,), (1,)), ((), ())), preferred_element_type=jnp.float32
    )


def contract_first(left, right):
    return lax.dot_general(
        left, right, (((0,), (0,)), ((), ())), preferred_element_type=jnp.float32
    )


def gather_rows(block, axis, count):
    tiled = jnp.tile(block, (count, 1))
    return lax.all_to_all(tiled, axis, 0, 0, tiled=True)


def scatter_sum_rows(partial, axis, count):
    received = lax.all_to_all(partial.astype(jnp.bfloat16), axis, 0, 0, tiled=True)
    received = received.reshape((count, partial.shape[0] // count) + partial.shape[1:])
    return received.astype(jnp.float32).sum(0)


def sum_all(partial, axis, count):
    total = scatter_sum_rows(partial, axis, count)
    return gather_rows(total.astype(jnp.bfloat16), axis, count).astype(jnp.float32)


def make_body(rows, cols):
    def body(inputs, out_grad, gate_pre, up_pre, gate_weight, up_weight, down_weight):
        grad_rows = gather_rows(out_grad, "row", rows)
        width = gate_pre.shape[1]
        pre_all = lax.all_gather(
            jnp.concatenate([gate_pre, up_pre], axis=1), "col", axis=0, tiled=True
        )
        gate_all, up_all = pre_all[:, :width], pre_all[:, width:]
        partial_hidden = contract_last(grad_rows, down_weight)
        hidden_total = sum_all(partial_hidden, "col", cols)
        hidden, gate_grad, up_grad = swiglu_back(hidden_total, gate_all, up_all)
        grad_down = contract_first(hidden, grad_rows).astype(jnp.bfloat16)
        input_rows = gather_rows(inputs, "row", rows)
        gate_total = contract_first(input_rows, gate_grad)
        up_total = contract_first(input_rows, up_grad)
        input_total = scatter_sum_rows(
            contract_last(gate_grad, gate_weight) + contract_last(up_grad, up_weight),
            "row",
            rows,
        )
        return (
            input_total.astype(jnp.bfloat16),
            gate_total.astype(jnp.bfloat16),
            up_total.astype(jnp.bfloat16),
            grad_down,
        )

    return body


def solution(mesh):
    in_specs = (
        P("row", "col"),
        P("row", "col"),
        P("col", "row"),
        P("col", "row"),
        P("col", "row"),
        P("col", "row"),
        P("row", "col"),
    )
    out_specs = (P("row", "col"), P("col", "row"), P("col", "row"), P("row", "col"))
    body = make_body(mesh.shape["row"], mesh.shape["col"])
    return jax.shard_map(body, mesh=mesh, in_specs=in_specs, out_specs=out_specs, check_vma=False)
```

```python
import jax
import jax.numpy as jnp
from jax import lax
from jax.sharding import PartitionSpec as P


def swiglu_back(hidden_grad, gate_stored, up_stored):
    gate_value = gate_stored.astype(jnp.float32)
    up_value = up_stored.astype(jnp.float32)
    sigmoid_gate = jax.nn.sigmoid(gate_value)
    activated = gate_value * sigmoid_gate
    hidden = (activated * up_value).astype(jnp.bfloat16)
    gate_grad = (
        hidden_grad * up_value * sigmoid_gate * (1.0 + gate_value * (1.0 - sigmoid_gate))
    ).astype(jnp.bfloat16)
    up_grad = (hidden_grad * activated).astype(jnp.bfloat16)
    return (hidden, gate_grad, up_grad)


def contract_last(left, right):
    return lax.dot_general(
        left, right, (((1,), (1,)), ((), ())), preferred_element_type=jnp.float32
    )


def contract_first(left, right):
    return lax.dot_general(
        left, right, (((0,), (0,)), ((), ())), preferred_element_type=jnp.float32
    )


def gather_rows(block, axis, count):
    tiled = jnp.tile(block, (count, 1))
    return lax.all_to_all(tiled, axis, 0, 0, tiled=True)


def scatter_sum_rows(partial, axis, count):
    received = lax.all_to_all(partial.astype(jnp.bfloat16), axis, 0, 0, tiled=True)
    received = received.reshape((count, partial.shape[0] // count) + partial.shape[1:])
    return received.astype(jnp.float32).sum(0)


def sum_all(partial, axis, count):
    received = lax.all_to_all(partial, axis, 0, 0, tiled=True)
    total = received.reshape((count, partial.shape[0] // count) + partial.shape[1:]).sum(0)
    return gather_rows(total, axis, count)


def make_body(rows, cols):
    def body(inputs, out_grad, gate_pre, up_pre, gate_weight, up_weight, down_weight):
      grad_rows = gather_rows(out_grad, "row", rows)
      width = gate_pre.shape[1]
      pre_all = lax.all_gather(
          jnp.concatenate([gate_pre, up_pre], axis=1), "col", axis=0, tiled=True
      )
      gate_all, up_all = pre_all[:, :width], pre_all[:, width:]
      partial_hidden = contract_last(grad_rows, down_weight)
      hidden_total = sum_all(partial_hidden, "col", cols)
      hidden, gate_grad, up_grad = swiglu_back(hidden_total, gate_all, up_all)
      grad_down = contract_first(hidden, grad_rows).astype(jnp.bfloat16)
      input_rows = lax.all_gather(inputs, "row", axis=0, tiled=True)
      gate_total = contract_first(input_rows, gate_grad)
      up_total = contract_first(input_rows, up_grad)
      input_total = scatter_sum_rows(
          contract_last(gate_grad, gate_weight) + contract_last(up_grad, up_weight),
          "row",
          rows,
      )
      return (
          input_total.astype(jnp.bfloat16),
          gate_total.astype(jnp.bfloat16),
          up_total.astype(jnp.bfloat16),
          grad_down,
      )

    return body


def solution(mesh):
    in_specs = (
        P("row", "col"),
        P("row", "col"),
        P("col", "row"),
        P("col", "row"),
        P("col", "row"),
        P("col", "row"),
        P("row", "col"),
    )
    out_specs = (P("row", "col"), P("col", "row"), P("col", "row"), P("row", "col"))
    body = make_body(mesh.shape["row"], mesh.shape["col"])
    return jax.shard_map(body, mesh=mesh, in_specs=in_specs, out_specs=out_specs, check_vma=False)
```

```python
import jax
import jax.numpy as jnp
from jax import lax
from jax.sharding import PartitionSpec as P


def swiglu_back(hidden_grad, gate_stored, up_stored):
    gate_value = gate_stored.astype(jnp.float32)
    up_value = up_stored.astype(jnp.float32)
    sigmoid_gate = jax.nn.sigmoid(gate_value)
    activated = gate_value * sigmoid_gate
    hidden = (activated * up_value).astype(jnp.bfloat16)
    gate_grad = (
        hidden_grad * up_value * sigmoid_gate * (1.0 + gate_value * (1.0 - sigmoid_gate))
    ).astype(jnp.bfloat16)
    up_grad = (hidden_grad * activated).astype(jnp.bfloat16)
    return (hidden, gate_grad, up_grad)


def contract_last(left, right):
    return lax.dot_general(
        left, right, (((1,), (1,)), ((), ())), preferred_element_type=jnp.float32
    )


def contract_first(left, right):
    return lax.dot_general(
        left, right, (((0,), (0,)), ((), ())), preferred_element_type=jnp.float32
    )


def gather_rows(block, axis, count):
    tiled = jnp.tile(block, (count, 1))
    return lax.all_to_all(tiled, axis, 0, 0, tiled=True)


def scatter_sum_rows(partial, axis, count):
    received = lax.all_to_all(partial.astype(jnp.bfloat16), axis, 0, 0, tiled=True)
    received = received.reshape((count, partial.shape[0] // count) + partial.shape[1:])
    return received.astype(jnp.float32).sum(0)


def swap(value, axis, count, bit):
    pairs = [(i, i ^ bit) for i in range(count)]
    return lax.ppermute(value, axis, pairs)


def halve_sum(value, axis, count, bit, own):
    half = value.shape[0] // 2
    keep = lax.dynamic_slice_in_dim(value, own * half, half, axis=0)
    give = lax.dynamic_slice_in_dim(value, (1 - own) * half, half, axis=0)
    return keep + swap(give, axis, count, bit)


def double(value, axis, count, bit, own):
    other = swap(value, axis, count, bit)
    first = jnp.where(own == 0, value, other)
    second = jnp.where(own == 0, other, value)
    return jnp.concatenate([first, second], axis=0)


def sum_all(partial, axis, count):
    index = lax.axis_index(axis)
    near, far = index % 2, (index // 2) % 2
    total = halve_sum(partial, axis, count, 1, near)
    total = halve_sum(total, axis, count, 2, far)
    total = double(total, axis, count, 2, far)
    return double(total, axis, count, 1, near)


def make_body(rows, cols):
    def body(inputs, out_grad, gate_pre, up_pre, gate_weight, up_weight, down_weight):
      features = out_grad.shape[1]
      both_rows = gather_rows(jnp.concatenate([out_grad, inputs], axis=1), "row", rows)
      grad_rows, input_rows = both_rows[:, :features], both_rows[:, features:]
      width = gate_pre.shape[1]
      pre_all = lax.all_gather(
          jnp.concatenate([gate_pre, up_pre], axis=1), "col", axis=0, tiled=True
      )
      gate_all, up_all = pre_all[:, :width], pre_all[:, width:]
      partial_hidden = contract_last(grad_rows, down_weight)
      hidden_total = sum_all(partial_hidden, "col", cols)
      hidden, gate_grad, up_grad = swiglu_back(hidden_total, gate_all, up_all)
      grad_down = contract_first(hidden, grad_rows).astype(jnp.bfloat16)
      gate_total = contract_first(input_rows, gate_grad)
      up_total = contract_first(input_rows, up_grad)
      input_total = scatter_sum_rows(
          contract_last(gate_grad, gate_weight) + contract_last(up_grad, up_weight),
          "row",
          rows,
      )
      return (
          input_total.astype(jnp.bfloat16),
          gate_total.astype(jnp.bfloat16),
          up_total.astype(jnp.bfloat16),
          grad_down,
      )

    return body


def solution(mesh):
    in_specs = (
        P("row", "col"),
        P("row", "col"),
        P("col", "row"),
        P("col", "row"),
        P("col", "row"),
        P("col", "row"),
        P("row", "col"),
    )
    out_specs = (P("row", "col"), P("col", "row"), P("col", "row"), P("row", "col"))
    body = make_body(mesh.shape["row"], mesh.shape["col"])
    return jax.shard_map(body, mesh=mesh, in_specs=in_specs, out_specs=out_specs, check_vma=False)
```

```python
import jax
import jax.numpy as jnp
from jax import lax
from jax.sharding import PartitionSpec as P


def swiglu_back(hidden_grad, gate_stored, up_stored):
    gate_value = gate_stored.astype(jnp.float32)
    up_value = up_stored.astype(jnp.float32)
    sigmoid_gate = jax.nn.sigmoid(gate_value)
    activated = gate_value * sigmoid_gate
    hidden = (activated * up_value).astype(jnp.bfloat16)
    gate_grad = (
        hidden_grad * up_value * sigmoid_gate * (1.0 + gate_value * (1.0 - sigmoid_gate))
    ).astype(jnp.bfloat16)
    up_grad = (hidden_grad * activated).astype(jnp.bfloat16)
    return (hidden, gate_grad, up_grad)


def contract_last(left, right):
    return lax.dot_general(
        left, right, (((1,), (1,)), ((), ())), preferred_element_type=jnp.float32
    )


def contract_first(left, right):
    return lax.dot_general(
        left, right, (((0,), (0,)), ((), ())), preferred_element_type=jnp.float32
    )


def gather_rows(block, axis, count):
    tiled = jnp.tile(block, (count, 1))
    return lax.all_to_all(tiled, axis, 0, 0, tiled=True)


def scatter_sum_rows(partial, axis, count):
    received = lax.all_to_all(partial.astype(jnp.bfloat16), axis, 0, 0, tiled=True)
    received = received.reshape((count, partial.shape[0] // count) + partial.shape[1:])
    return received.astype(jnp.float32).sum(0)


def swap(value, axis, count, bit):
    pairs = [(i, i ^ bit) for i in range(count)]
    return lax.ppermute(value, axis, pairs)


def halve_sum(value, axis, count, bit, own):
    half = value.shape[0] // 2
    keep = lax.dynamic_slice_in_dim(value, own * half, half, axis=0)
    give = lax.dynamic_slice_in_dim(value, (1 - own) * half, half, axis=0)
    return keep + swap(give, axis, count, bit)


def double(value, axis, count, bit, own):
    other = swap(value, axis, count, bit)
    first = jnp.where(own == 0, value, other)
    second = jnp.where(own == 0, other, value)
    return jnp.concatenate([first, second], axis=0)


def sum_all(partial, axis, count):
    index = lax.axis_index(axis)
    near, far = index % 2, (index // 2) % 2
    total = halve_sum(partial, axis, count, 1, near)
    total = halve_sum(total, axis, count, 2, far)
    total = double(total, axis, count, 2, far)
    return double(total, axis, count, 1, near)


def make_body(rows, cols):
    def body(inputs, out_grad, gate_pre, up_pre, gate_weight, up_weight, down_weight):
      grad_rows = gather_rows(out_grad, "row", rows)
      width = gate_pre.shape[1]
      pre_all = lax.all_gather(
          jnp.concatenate([gate_pre, up_pre], axis=1), "col", axis=0, tiled=True
      )
      gate_all, up_all = pre_all[:, :width], pre_all[:, width:]
      partial_hidden = contract_last(grad_rows, down_weight)
      hidden_total = sum_all(partial_hidden, "col", cols)
      hidden, gate_grad, up_grad = swiglu_back(hidden_total, gate_all, up_all)
      grad_down = contract_first(hidden, grad_rows).astype(jnp.bfloat16)
      input_rows = lax.all_gather(inputs, "row", axis=0, tiled=True)
      gate_total = contract_first(input_rows, gate_grad)
      up_total = contract_first(input_rows, up_grad)
      input_total = scatter_sum_rows(
          contract_last(gate_grad, gate_weight) + contract_last(up_grad, up_weight),
          "row",
          rows,
      )
      return (
          input_total.astype(jnp.bfloat16),
          gate_total.astype(jnp.bfloat16),
          up_total.astype(jnp.bfloat16),
          grad_down,
      )

    return body


def solution(mesh):
    in_specs = (
        P("row", "col"),
        P("row", "col"),
        P("col", "row"),
        P("col", "row"),
        P("col", "row"),
        P("col", "row"),
        P("row", "col"),
    )
    out_specs = (P("row", "col"), P("col", "row"), P("col", "row"), P("row", "col"))
    body = make_body(mesh.shape["row"], mesh.shape["col"])
    return jax.shard_map(body, mesh=mesh, in_specs=in_specs, out_specs=out_specs, check_vma=False)
```

```python
import jax
import jax.numpy as jnp
from jax import lax
from jax.sharding import PartitionSpec as P


def swiglu_back(hidden_grad, gate_stored, up_stored):
    gate_value = gate_stored.astype(jnp.float32)
    up_value = up_stored.astype(jnp.float32)
    sigmoid_gate = jax.nn.sigmoid(gate_value)
    activated = gate_value * sigmoid_gate
    hidden = (activated * up_value).astype(jnp.bfloat16)
    gate_grad = (
        hidden_grad * up_value * sigmoid_gate * (1.0 + gate_value * (1.0 - sigmoid_gate))
    ).astype(jnp.bfloat16)
    up_grad = (hidden_grad * activated).astype(jnp.bfloat16)
    return (hidden, gate_grad, up_grad)


def contract_last(left, right):
    return lax.dot_general(
        left, right, (((1,), (1,)), ((), ())), preferred_element_type=jnp.float32
    )


def contract_first(left, right):
    return lax.dot_general(
        left, right, (((0,), (0,)), ((), ())), preferred_element_type=jnp.float32
    )


def gather_rows(block, axis, count):
    tiled = jnp.tile(block, (count, 1))
    return lax.all_to_all(tiled, axis, 0, 0, tiled=True)


def scatter_sum_rows(partial, axis, count):
    received = lax.all_to_all(partial.astype(jnp.bfloat16), axis, 0, 0, tiled=True)
    received = received.reshape((count, partial.shape[0] // count) + partial.shape[1:])
    return received.astype(jnp.float32).sum(0)


def swap(value, axis, count, bit, pieces=1):
    pairs = [(i, i ^ bit) for i in range(count)]
    parts = jnp.split(value, pieces, axis=0)
    return jnp.concatenate([lax.ppermute(part, axis, pairs) for part in parts], axis=0)


def halve_sum(value, axis, count, bit, own, pieces=1):
    half = value.shape[0] // 2
    keep = lax.dynamic_slice_in_dim(value, own * half, half, axis=0)
    give = lax.dynamic_slice_in_dim(value, (1 - own) * half, half, axis=0)
    return keep + swap(give, axis, count, bit, pieces)


def double(value, axis, count, bit, own, pieces=1):
    other = swap(value, axis, count, bit, pieces)
    first = jnp.where(own == 0, value, other)
    second = jnp.where(own == 0, other, value)
    return jnp.concatenate([first, second], axis=0)


def sum_all(partial, axis, count):
    index = lax.axis_index(axis)
    near, far = index % 2, (index // 2) % 2
    total = halve_sum(partial, axis, count, 1, near)
    total = halve_sum(total, axis, count, 2, far, 4)
    total = double(total, axis, count, 2, far, 4)
    return double(total, axis, count, 1, near)


def make_body(rows, cols):
    def body(inputs, out_grad, gate_pre, up_pre, gate_weight, up_weight, down_weight):
      grad_rows = gather_rows(out_grad, "row", rows)
      width = gate_pre.shape[1]
      pre_all = lax.all_gather(
          jnp.concatenate([gate_pre, up_pre], axis=1), "col", axis=0, tiled=True
      )
      gate_all, up_all = pre_all[:, :width], pre_all[:, width:]
      partial_hidden = contract_last(grad_rows, down_weight)
      hidden_total = sum_all(partial_hidden, "col", cols)
      hidden, gate_grad, up_grad = swiglu_back(hidden_total, gate_all, up_all)
      grad_down = contract_first(hidden, grad_rows).astype(jnp.bfloat16)
      input_rows = lax.all_gather(inputs, "row", axis=0, tiled=True)
      gate_total = contract_first(input_rows, gate_grad)
      up_total = contract_first(input_rows, up_grad)
      input_total = scatter_sum_rows(
          contract_last(gate_grad, gate_weight) + contract_last(up_grad, up_weight),
          "row",
          rows,
      )
      return (
          input_total.astype(jnp.bfloat16),
          gate_total.astype(jnp.bfloat16),
          up_total.astype(jnp.bfloat16),
          grad_down,
      )

    return body


def solution(mesh):
    in_specs = (
        P("row", "col"),
        P("row", "col"),
        P("col", "row"),
        P("col", "row"),
        P("col", "row"),
        P("col", "row"),
        P("row", "col"),
    )
    out_specs = (P("row", "col"), P("col", "row"), P("col", "row"), P("row", "col"))
    body = make_body(mesh.shape["row"], mesh.shape["col"])
    return jax.shard_map(body, mesh=mesh, in_specs=in_specs, out_specs=out_specs, check_vma=False)
```

```python
import jax
import jax.numpy as jnp
from jax import lax
from jax.sharding import Mesh, PartitionSpec as P


def swiglu_back(hidden_grad, gate_stored, up_stored):
    gate_value = gate_stored.astype(jnp.float32)
    up_value = up_stored.astype(jnp.float32)
    sigmoid_gate = jax.nn.sigmoid(gate_value)
    activated = gate_value * sigmoid_gate
    hidden = (activated * up_value).astype(jnp.bfloat16)
    gate_grad = (
        hidden_grad * up_value * sigmoid_gate * (1.0 + gate_value * (1.0 - sigmoid_gate))
    ).astype(jnp.bfloat16)
    up_grad = (hidden_grad * activated).astype(jnp.bfloat16)
    return (hidden, gate_grad, up_grad)


def contract_last(left, right):
    return lax.dot_general(
        left, right, (((1,), (1,)), ((), ())), preferred_element_type=jnp.float32
    )


def contract_first(left, right):
    return lax.dot_general(
        left, right, (((0,), (0,)), ((), ())), preferred_element_type=jnp.float32
    )


def gather_rows(block, axis, count):
    tiled = jnp.tile(block, (count, 1))
    return lax.all_to_all(tiled, axis, 0, 0, tiled=True)


def scatter_sum_rows(partial, axis, count):
    received = lax.all_to_all(partial.astype(jnp.bfloat16), axis, 0, 0, tiled=True)
    received = received.reshape((count, partial.shape[0] // count) + partial.shape[1:])
    return received.astype(jnp.float32).sum(0)


def swap(value, axis, count, bit):
    pairs = [(i, i ^ bit) for i in range(count)]
    return lax.ppermute(value, axis, pairs)


def halve_sum(value, axis, count, bit, own):
    half = value.shape[0] // 2
    keep = lax.dynamic_slice_in_dim(value, own * half, half, axis=0)
    give = lax.dynamic_slice_in_dim(value, (1 - own) * half, half, axis=0)
    return keep + swap(give, axis, count, bit)


def double(value, axis, count, bit, own):
    other = swap(value, axis, count, bit)
    first = jnp.where(own == 0, value, other)
    second = jnp.where(own == 0, other, value)
    return jnp.concatenate([first, second], axis=0)


def sum_all(partial, axis, count):
    index = lax.axis_index(axis)
    near, far = index % 2, (index // 2) % 2
    total = halve_sum(partial, axis, count, 1, near)
    total = halve_sum(total, axis, count, 2, far)
    total = double(total, axis, count, 2, far)
    return double(total, axis, count, 1, near)


ROW_PARTS = ("row_a", "row_b", "row_c")
COL_PARTS = ("col_a", "col_b")


def make_body(rows, cols):
    def body(inputs, out_grad, gate_pre, up_pre, gate_weight, up_weight, down_weight):
      grad_rows = gather_rows(out_grad, ROW_PARTS, rows)
      width = gate_pre.shape[1]
      pre_all = lax.all_gather(
          jnp.concatenate([gate_pre, up_pre], axis=1), COL_PARTS, axis=0, tiled=True
      )
      gate_all, up_all = pre_all[:, :width], pre_all[:, width:]
      partial_hidden = contract_last(grad_rows, down_weight)
      hidden_total = sum_all(partial_hidden, COL_PARTS, cols)
      hidden, gate_grad, up_grad = swiglu_back(hidden_total, gate_all, up_all)
      grad_down = contract_first(hidden, grad_rows).astype(jnp.bfloat16)
      input_rows = inputs
      for part in reversed(ROW_PARTS):
          input_rows = lax.all_gather(input_rows, part, axis=0, tiled=True)
      gate_total = contract_first(input_rows, gate_grad)
      up_total = contract_first(input_rows, up_grad)
      input_total = scatter_sum_rows(
          contract_last(gate_grad, gate_weight) + contract_last(up_grad, up_weight),
          ROW_PARTS,
          rows,
      )
      return (
          input_total.astype(jnp.bfloat16),
          gate_total.astype(jnp.bfloat16),
          up_total.astype(jnp.bfloat16),
          grad_down,
      )

    return body


def solution(mesh):
    in_specs = (
        P("row", "col"),
        P("row", "col"),
        P("col", "row"),
        P("col", "row"),
        P("col", "row"),
        P("col", "row"),
        P("row", "col"),
    )
    out_specs = (P("row", "col"), P("col", "row"), P("col", "row"), P("row", "col"))
    body = make_body(mesh.shape["row"], mesh.shape["col"])
    fine = Mesh(mesh.devices.reshape(2, mesh.shape["row"] // 8, 4, 2, mesh.shape["col"] // 2), ROW_PARTS + COL_PARTS)
    in_specs = tuple(P(*(ROW_PARTS if a == "row" else COL_PARTS for a in spec)) for spec in in_specs)
    out_specs = tuple(P(*(ROW_PARTS if a == "row" else COL_PARTS for a in spec)) for spec in out_specs)
    return jax.shard_map(body, mesh=fine, in_specs=in_specs, out_specs=out_specs, check_vma=False)
```

```python
import jax
import jax.numpy as jnp
from jax import lax
from jax.experimental.layout import Layout, with_layout_constraint
from jax.sharding import PartitionSpec as P


def swiglu_back(hidden_grad, gate_stored, up_stored):
    gate_value = gate_stored.astype(jnp.float32)
    up_value = up_stored.astype(jnp.float32)
    sigmoid_gate = jax.nn.sigmoid(gate_value)
    activated = gate_value * sigmoid_gate
    hidden = (activated * up_value).astype(jnp.bfloat16)
    gate_grad = (
        hidden_grad * up_value * sigmoid_gate * (1.0 + gate_value * (1.0 - sigmoid_gate))
    ).astype(jnp.bfloat16)
    up_grad = (hidden_grad * activated).astype(jnp.bfloat16)
    return (hidden, gate_grad, up_grad)


def contract_last(left, right):
    return lax.dot_general(
        left, right, (((1,), (1,)), ((), ())), preferred_element_type=jnp.float32
    )


def contract_first(left, right):
    return lax.dot_general(
        left, right, (((0,), (0,)), ((), ())), preferred_element_type=jnp.float32
    )


def gather_rows(block, axis, count):
    tiled = jnp.tile(block, (count, 1))
    return lax.all_to_all(tiled, axis, 0, 0, tiled=True)


def scatter_sum_rows(partial, axis, count):
    received = lax.all_to_all(partial.astype(jnp.bfloat16), axis, 0, 0, tiled=True)
    received = received.reshape((count, partial.shape[0] // count) + partial.shape[1:])
    return received.astype(jnp.float32).sum(0)


def swap(value, axis, count, bit):
    pairs = [(i, i ^ bit) for i in range(count)]
    return lax.ppermute(value, axis, pairs)


def halve_sum(value, axis, count, bit, own):
    half = value.shape[0] // 2
    keep = lax.dynamic_slice_in_dim(value, own * half, half, axis=0)
    give = lax.dynamic_slice_in_dim(value, (1 - own) * half, half, axis=0)
    return keep + swap(give, axis, count, bit)


def double(value, axis, count, bit, own):
    other = swap(value, axis, count, bit)
    first = jnp.where(own == 0, value, other)
    second = jnp.where(own == 0, other, value)
    return jnp.concatenate([first, second], axis=0)


def sum_all(partial, axis, count):
    index = lax.axis_index(axis)
    near, far = index % 2, (index // 2) % 2
    total = halve_sum(partial, axis, count, 1, near)
    total = halve_sum(total, axis, count, 2, far)
    total = double(total, axis, count, 2, far)
    return double(total, axis, count, 1, near)


def make_body(rows, cols):
    def body(inputs, out_grad, gate_pre, up_pre, gate_weight, up_weight, down_weight):
      grad_rows = gather_rows(out_grad, "row", rows)
      width = gate_pre.shape[1]
      pre_all = lax.all_gather(
          jnp.concatenate([gate_pre, up_pre], axis=1), "col", axis=0, tiled=True
      )
      gate_all, up_all = pre_all[:, :width], pre_all[:, width:]
      partial_hidden = contract_last(grad_rows, down_weight)
      hidden_total = sum_all(partial_hidden, "col", cols)
      hidden, gate_grad, up_grad = swiglu_back(hidden_total, gate_all, up_all)
      grad_down = contract_first(hidden, grad_rows).astype(jnp.bfloat16)
      input_rows = lax.all_gather(inputs, "row", axis=0, tiled=True)
      row_major = Layout(major_to_minor=(0, 1))
      gate_total = with_layout_constraint(contract_first(input_rows, gate_grad), row_major)
      up_total = with_layout_constraint(contract_first(input_rows, up_grad), row_major)
      input_total = scatter_sum_rows(
          contract_last(gate_grad, gate_weight) + contract_last(up_grad, up_weight),
          "row",
          rows,
      )
      return (
          input_total.astype(jnp.bfloat16),
          gate_total.astype(jnp.bfloat16),
          up_total.astype(jnp.bfloat16),
          grad_down,
      )

    return body


def solution(mesh):
    in_specs = (
        P("row", "col"),
        P("row", "col"),
        P("col", "row"),
        P("col", "row"),
        P("col", "row"),
        P("col", "row"),
        P("row", "col"),
    )
    out_specs = (P("row", "col"), P("col", "row"), P("col", "row"), P("row", "col"))
    body = make_body(mesh.shape["row"], mesh.shape["col"])
    return jax.shard_map(body, mesh=mesh, in_specs=in_specs, out_specs=out_specs, check_vma=False)
```

```python
import jax
import jax.numpy as jnp
from jax import lax
from jax.experimental.layout import Layout, with_layout_constraint
from jax.sharding import PartitionSpec as P


def swiglu_back(hidden_grad, gate_stored, up_stored):
    gate_value = gate_stored.astype(jnp.float32)
    up_value = up_stored.astype(jnp.float32)
    sigmoid_gate = jax.nn.sigmoid(gate_value)
    activated = gate_value * sigmoid_gate
    hidden = (activated * up_value).astype(jnp.bfloat16)
    gate_grad = (
        hidden_grad * up_value * sigmoid_gate * (1.0 + gate_value * (1.0 - sigmoid_gate))
    ).astype(jnp.bfloat16)
    up_grad = (hidden_grad * activated).astype(jnp.bfloat16)
    return (hidden, gate_grad, up_grad)


def contract_last(left, right):
    return lax.dot_general(
        left, right, (((1,), (1,)), ((), ())), preferred_element_type=jnp.float32
    )


def contract_first(left, right):
    return lax.dot_general(
        left, right, (((0,), (0,)), ((), ())), preferred_element_type=jnp.float32
    )


def gather_rows(block, axis, count):
    tiled = jnp.tile(block, (count, 1))
    return lax.all_to_all(tiled, axis, 0, 0, tiled=True)


def scatter_sum_rows(partial, axis, count):
    received = lax.all_to_all(partial.astype(jnp.bfloat16), axis, 0, 0, tiled=True)
    received = received.reshape((count, partial.shape[0] // count) + partial.shape[1:])
    return received.astype(jnp.float32).sum(0)


def swap(value, axis, count, bit):
    pairs = [(i, i ^ bit) for i in range(count)]
    return lax.ppermute(value, axis, pairs)


def halve_sum(value, axis, count, bit, own):
    half = value.shape[0] // 2
    keep = lax.dynamic_slice_in_dim(value, own * half, half, axis=0)
    give = lax.dynamic_slice_in_dim(value, (1 - own) * half, half, axis=0)
    return keep + swap(give, axis, count, bit)


def double(value, axis, count, bit, own):
    other = swap(value, axis, count, bit)
    half = value.shape[0]
    whole = jnp.concatenate([value, value], axis=0)
    return lax.dynamic_update_slice_in_dim(whole, other, (1 - own) * half, axis=0)


def sum_all(partial, axis, count):
    index = lax.axis_index(axis)
    near, far = index % 2, (index // 2) % 2
    total = halve_sum(partial, axis, count, 1, near)
    total = halve_sum(total, axis, count, 2, far)
    total = double(total, axis, count, 2, far)
    return double(total, axis, count, 1, near)


def make_body(rows, cols):
    def body(inputs, out_grad, gate_pre, up_pre, gate_weight, up_weight, down_weight):
      grad_rows = gather_rows(out_grad, "row", rows)
      width = gate_pre.shape[1]
      pre_all = lax.all_gather(
          jnp.concatenate([gate_pre, up_pre], axis=1), "col", axis=0, tiled=True
      )
      gate_all, up_all = pre_all[:, :width], pre_all[:, width:]
      partial_hidden = contract_last(grad_rows, down_weight)
      hidden_total = sum_all(partial_hidden, "col", cols)
      hidden, gate_grad, up_grad = swiglu_back(hidden_total, gate_all, up_all)
      grad_down = contract_first(hidden, grad_rows).astype(jnp.bfloat16)
      input_rows = lax.all_gather(inputs, "row", axis=0, tiled=True)
      row_major = Layout(major_to_minor=(0, 1))
      gate_total = with_layout_constraint(contract_first(input_rows, gate_grad), row_major)
      up_total = with_layout_constraint(contract_first(input_rows, up_grad), row_major)
      input_total = scatter_sum_rows(
          contract_last(gate_grad, gate_weight) + contract_last(up_grad, up_weight),
          "row",
          rows,
      )
      return (
          input_total.astype(jnp.bfloat16),
          gate_total.astype(jnp.bfloat16),
          up_total.astype(jnp.bfloat16),
          grad_down,
      )

    return body


def solution(mesh):
    in_specs = (
        P("row", "col"),
        P("row", "col"),
        P("col", "row"),
        P("col", "row"),
        P("col", "row"),
        P("col", "row"),
        P("row", "col"),
    )
    out_specs = (P("row", "col"), P("col", "row"), P("col", "row"), P("row", "col"))
    body = make_body(mesh.shape["row"], mesh.shape["col"])
    return jax.shard_map(body, mesh=mesh, in_specs=in_specs, out_specs=out_specs, check_vma=False)
```
